256 devices in a mesh: row: 8 (over x, core), col: 32 (over y, z).
Axes of the slice: x: 4, y: 4, z: 8, core: 2. Of those that a mesh axis runs over, the one named last changes fastest.
Arguments:
- features: bfloat16 [262144, 256], P(('row', 'col')), may hold values from -6 to 6
- weight: bfloat16 [256, 256], replicated, may hold values from -0.375 to 0.375
- layer_bias: float32 [256], replicated, may hold values from -3 to 3
- adj_tiles: bfloat16 [12288, 128, 128], P(('row', 'col')), may hold values from 0 to 0.079589844
- tile_source: int32 [12288], P(('row', 'col')), may hold values from 0 to 23, as said below
- tile_target: int32 [12288], P(('row', 'col')), may hold values from 0 to 95, as said below
- tile_count: int32 [256], P(('row', 'col')), may hold values from 1 to 48, as said below
- fetch_list: int32 [2048, 3], P(('row', 'col')), may hold values from -1 to 7, as said below
- deliver_list: int32 [8192, 3], P(('row', 'col')), may hold values from -1 to 7, as said below
- cotangent: bfloat16 [262144, 256], P(('row', 'col')), may hold values from -6 to 6
Outputs:
- layer_out: bfloat16 [262144, 256], P(('row', 'col'))
- grad_features: bfloat16 [262144, 256], P(('row', 'col'))
- grad_weight: float32 [256, 256], replicated
- grad_bias: float32 [256], replicated
The draws below stay inside these ranges and needn't reach their ends.
Inputs may be any that keep to these rules, and one draw needn't show every extreme that they name: `tile_source`: each entry names a source slot q * 3 + j of its device whose fetch_list entry is not -1. `tile_target`: each entry names a row slot p * 3 + j of its device whose deliver_list entry is not -1. `tile_count`: live tiles are the first ones of a device; in every draw some device has 48 live tiles. `fetch_list`: each list holds one or more distinct local block numbers, then -1 in its unused slots; in every draw some device has all its lists full. `deliver_list`: each list holds one or more distinct local block numbers, then -1 in its unused slots; in every draw some owner has all its lists full.
All inputs are finite; a program needn't handle non-finite values.
Results may differ from the reference program's by a relative error of at most 0.0085.
Values may be sent and summed in bfloat16 or wider, within the bound.
No kernel may reach another device: no remote copies, remote signals or barrier semaphores. Data moves between devices by JAX's collectives and lax.ppermute only.
A program may use at most 128 MiB of HBM per device.

```python
import jax
import jax.numpy as jnp
from jax import lax

F = 256
TILE = 128
BLK_DEV = 8
TILES_DEV = 48
CAPF = 3
CAPO = 3
GRID_ROWS = 8
GRID_COLS = 32
MESH_DEVICES = 256
NODES = 262144
SRC_SLOTS = 24
ROW_SLOTS = 96


def distinct_blocks(lists_key, rows_total, capacity):
    scores = jax.random.randint(lists_key, (rows_total, BLK_DEV), 0, 1 << 20)
    scores = scores * BLK_DEV + jnp.arange(BLK_DEV, dtype=jnp.int32)[None, :]
    ranking = jnp.argsort(scores, axis=1, stable=True)
    return ranking[:, :capacity].astype(jnp.int32)


def fetch_tables(key):
    lists_key = jax.random.fold_in(key, 11)
    rows_total = MESH_DEVICES * GRID_ROWS
    lengths = jax.random.randint(jax.random.fold_in(lists_key, 1), (rows_total,), 1, CAPF + 1)
    chosen = jax.random.randint(jax.random.fold_in(lists_key, 2), (), 0, MESH_DEVICES)
    row_owner = jnp.arange(rows_total, dtype=jnp.int32) // GRID_ROWS
    lengths = jnp.where(row_owner == chosen, CAPF, lengths).astype(jnp.int32)
    entries = distinct_blocks(jax.random.fold_in(lists_key, 3), rows_total, CAPF)
    listing = jnp.where(jnp.arange(CAPF, dtype=jnp.int32)[None, :] < lengths[:, None], entries, -1)
    return (listing.astype(jnp.int32), lengths, chosen)


def deliver_tables(key):
    lists_key = jax.random.fold_in(key, 12)
    rows_total = MESH_DEVICES * GRID_COLS
    lengths = jax.random.randint(jax.random.fold_in(lists_key, 1), (rows_total,), 1, CAPO + 1)
    chosen_row = jax.random.randint(jax.random.fold_in(lists_key, 2), (), 0, GRID_ROWS)
    chosen = chosen_row * GRID_COLS + GRID_COLS - 1
    row_owner = jnp.arange(rows_total, dtype=jnp.int32) // GRID_COLS
    lengths = jnp.where(row_owner == chosen, CAPO, lengths).astype(jnp.int32)
    entries = distinct_blocks(jax.random.fold_in(lists_key, 3), rows_total, CAPO)
    listing = jnp.where(jnp.arange(CAPO, dtype=jnp.int32)[None, :] < lengths[:, None], entries, -1)
    return (listing.astype(jnp.int32), lengths, chosen_row)


def draw_fetch_list(key, part):
    tables = fetch_tables(key)
    return tables[0]


def draw_deliver_list(key, part):
    tables = deliver_tables(key)
    return tables[0]


def draw_tile_source(key, part):
    tables = fetch_tables(key)
    lengths = tables[1]
    chosen = tables[2]
    device_ids = jnp.arange(MESH_DEVICES, dtype=jnp.int32)[:, None]
    owners = jax.random.randint(jax.random.fold_in(key, 21), (MESH_DEVICES, TILES_DEV), 0, GRID_ROWS)
    raw_bits = jax.random.randint(jax.random.fold_in(key, 22), (MESH_DEVICES, TILES_DEV), 0, 1 << 20)
    available = lengths[device_ids * GRID_ROWS + owners]
    slots = owners * CAPF + raw_bits % available
    positions = jnp.arange(TILES_DEV, dtype=jnp.int32)[None, :]
    slots = jnp.where((device_ids == chosen) & (positions == 0), SRC_SLOTS - 1, slots)
    slots = jnp.where((device_ids == chosen) & (positions == 1), 0, slots)
    return slots.reshape(-1).astype(jnp.int32)


def draw_tile_target(key, part):
    tables = deliver_tables(key)
    lengths = tables[1]
    chosen_row = tables[2]
    device_ids = jnp.arange(MESH_DEVICES, dtype=jnp.int32)[:, None]
    grid_row = device_ids // GRID_COLS
    grid_col = device_ids % GRID_COLS
    owners = jax.random.randint(jax.random.fold_in(key, 23), (MESH_DEVICES, TILES_DEV), 0, GRID_COLS)
    raw_bits = jax.random.randint(jax.random.fold_in(key, 24), (MESH_DEVICES, TILES_DEV), 0, 1 << 20)
    available = lengths[(grid_row * GRID_COLS + owners) * GRID_COLS + grid_col]
    slots = owners * CAPO + raw_bits % available
    positions = jnp.arange(TILES_DEV, dtype=jnp.int32)[None, :]
    marked = device_ids == chosen_row * GRID_COLS
    slots = jnp.where(marked & (positions == 0), ROW_SLOTS - 1, slots)
    slots = jnp.where(marked & (positions == 1), 0, slots)
    return slots.reshape(-1).astype(jnp.int32)


def draw_tile_count(key, part):
    halvings = jax.random.randint(jax.random.fold_in(key, 31), (MESH_DEVICES,), 0, 4)
    base_count = jnp.right_shift(jnp.int32(TILES_DEV), halvings)
    spread = jnp.maximum(1, jnp.right_shift(jnp.int32(TILES_DEV), halvings + 2))
    jitter = jax.random.randint(jax.random.fold_in(key, 32), (MESH_DEVICES,), 0, 1 << 20) % spread
    counts = base_count - jitter
    chosen = jax.random.randint(jax.random.fold_in(key, 33), (), 0, MESH_DEVICES)
    counts = jnp.where(jnp.arange(MESH_DEVICES, dtype=jnp.int32) == chosen, TILES_DEV, counts)
    return counts.astype(jnp.int32)


def block_levels(rng, shape, pieces, least, top_value):
    loudness = 1.0
    for dim, shards_of in pieces:
        steps = jax.random.uniform(jax.random.fold_in(jax.random.fold_in(rng, 6), dim), (shards_of,), jnp.float32, least / len(pieces), top_value / len(pieces))
        loudness = loudness * jnp.repeat(jnp.exp(steps), shape[dim] // shards_of).reshape((-1,) + (1,) * (len(shape) - 1 - dim))
    return loudness


def scatter_about(own_key, dims, scale, reach, split=(), kind=jnp.bfloat16):
    drawn = jax.random.normal(own_key, dims, jnp.float32) * scale
    if len(split) > 0:
        drawn = block_levels(own_key, dims, split, -0.22, 0.18) * drawn
    return jnp.clip(drawn, min=-reach, max=reach).astype(kind)


def setup_inputs(seed: int = 0) -> dict:
    key_of = jax.random.split(jax.random.key(seed), 11)
    return {
        "features": scatter_about(key_of[0], (NODES, F), 1.0, 6.0, ((0, 256),)),
        "weight": scatter_about(key_of[1], (F, F), F ** -0.5, 0.375),
        "layer_bias": scatter_about(key_of[2], (F,), 0.5, 3.0, (), jnp.float32),
        "adj_tiles": jnp.clip(0.079589844 * jax.random.uniform(key_of[3], (MESH_DEVICES * TILES_DEV, TILE, TILE), jnp.float32) ** block_levels(key_of[3], (MESH_DEVICES * TILES_DEV, TILE, TILE), ((0, 256),), -0.2, 0.2), 0.0, 0.079589844).astype(jnp.bfloat16),
        "tile_source": draw_tile_source(jax.random.fold_in(key_of[10], 71), 0),
        "tile_target": draw_tile_target(jax.random.fold_in(key_of[10], 71), 0),
        "tile_count": draw_tile_count(jax.random.fold_in(key_of[10], 71), 0),
        "fetch_list": draw_fetch_list(jax.random.fold_in(key_of[10], 71), 0),
        "deliver_list": draw_deliver_list(jax.random.fold_in(key_of[10], 71), 0),
        "cotangent": scatter_about(key_of[9], (NODES, F), 1.0, 6.0, ((0, 256),)),
    }


def silu_grad(values):
    logistic = jax.nn.sigmoid(values)
    return logistic * (1.0 + values * (1.0 - logistic))

def slot_blocks(fetch_list, deliver_list):
    device_ids = jnp.arange(MESH_DEVICES, dtype=jnp.int32)
    grid_row = device_ids // GRID_COLS
    grid_col = device_ids % GRID_COLS
    src_owner = jnp.arange(GRID_ROWS, dtype=jnp.int32)[None, :] * GRID_COLS + grid_col[:, None]
    src_entry = fetch_list.reshape(MESH_DEVICES, GRID_ROWS, CAPF)
    src_block = jnp.where(src_entry >= 0, src_owner[:, :, None] * BLK_DEV + src_entry, -1)
    row_owner = grid_row[:, None] * GRID_COLS + jnp.arange(GRID_COLS, dtype=jnp.int32)[None, :]
    row_entry = deliver_list[row_owner * GRID_COLS + grid_col[:, None]]
    row_block = jnp.where(row_entry >= 0, row_owner[:, :, None] * BLK_DEV + row_entry, -1)
    return (src_block.reshape(MESH_DEVICES, SRC_SLOTS).astype(jnp.int32), row_block.reshape(MESH_DEVICES, ROW_SLOTS).astype(jnp.int32))

def reference(features, weight, layer_bias, adj_tiles, tile_source, tile_target, tile_count, fetch_list, deliver_list, cotangent):
    block_total = NODES // TILE
    projected = jnp.dot(features, weight, preferred_element_type=jnp.float32).astype(jnp.bfloat16)
    proj_blocks = projected.reshape(block_total, TILE, F)
    src_block, row_block = slot_blocks(fetch_list, deliver_list)
    tile_sets = adj_tiles.reshape(MESH_DEVICES, TILES_DEV, TILE, TILE)
    sources = tile_source.reshape(MESH_DEVICES, TILES_DEV)
    targets = tile_target.reshape(MESH_DEVICES, TILES_DEV)
    positions = jnp.arange(TILES_DEV, dtype=jnp.int32)
    device_items = (tile_sets, sources, targets, tile_count, src_block, row_block)

    def forward_step(running, device_item):
        tile_set, source, target, live_count, src_ids, row_ids = device_item
        picked = proj_blocks[jnp.maximum(src_ids[source], 0)].astype(jnp.float32)
        products = jnp.einsum('kij,kjf->kif', tile_set.astype(jnp.float32), picked)
        products = jnp.where((positions < live_count)[:, None, None], products, jnp.zeros_like(products))
        slot_sums = jax.ops.segment_sum(products, target, num_segments=ROW_SLOTS)
        slot_sums = lax.optimization_barrier(slot_sums.astype(jnp.bfloat16)).astype(jnp.float32)
        where_to = jnp.where(row_ids >= 0, row_ids, block_total).astype(jnp.int32)
        return (running.at[where_to].add(slot_sums, mode='drop'), None)
    aggregated, unused = lax.scan(forward_step, jnp.zeros((block_total, TILE, F), jnp.float32), device_items)
    pre_act = aggregated.reshape(NODES, F) + layer_bias
    layer_out = jax.nn.silu(pre_act).astype(jnp.bfloat16)
    slopes = cotangent.astype(jnp.float32) * silu_grad(pre_act)
    slope_blocks = slopes.astype(jnp.bfloat16).reshape(block_total, TILE, F)

    def backward_step(running, device_item):
        tile_set, source, target, live_count, src_ids, row_ids = device_item
        picked = slope_blocks[jnp.maximum(row_ids[target], 0)].astype(jnp.float32)
        products = jnp.einsum('kji,kjf->kif', tile_set.astype(jnp.float32), picked)
        products = jnp.where((positions < live_count)[:, None, None], products, jnp.zeros_like(products))
        slot_sums = jax.ops.segment_sum(products, source, num_segments=SRC_SLOTS)
        slot_sums = lax.optimization_barrier(slot_sums.astype(jnp.bfloat16)).astype(jnp.float32)
        where_to = jnp.where(src_ids >= 0, src_ids, block_total).astype(jnp.int32)
        return (running.at[where_to].add(slot_sums, mode='drop'), None)
    backward, unused = lax.scan(backward_step, jnp.zeros((block_total, TILE, F), jnp.float32), device_items)
    grad_proj = backward.reshape(NODES, F).astype(jnp.bfloat16)
    grad_features = jnp.dot(grad_proj, weight.T, preferred_element_type=jnp.float32).astype(jnp.bfloat16)
    grad_scale = NODES ** (-0.5)
    grad_weight = jnp.dot(features.T, grad_proj, preferred_element_type=jnp.float32) * grad_scale
    grad_bias = lax.optimization_barrier(jnp.sum(slopes, axis=0)) * grad_scale
    return (layer_out, grad_features, grad_weight, grad_bias)
```

```python
import math

import jax
import jax.numpy as jnp
from jax import lax
from jax.sharding import PartitionSpec as P


def silu_grad(values):
    logistic = jax.nn.sigmoid(values)
    return logistic * (1.0 + values * (1.0 - logistic))


def tile_sums(adj_tiles, operand, take_slot, put_slot, live_count, slot_total, transpose):
    pattern = "kji,kjf->kif" if transpose else "kij,kjf->kif"
    tile_total = adj_tiles.shape[0]
    live_mask = jnp.arange(tile_total, dtype=jnp.int32) < live_count
    products = jnp.einsum(
        pattern, adj_tiles, operand[take_slot], preferred_element_type=jnp.float32
    )
    products = jnp.where(live_mask[:, None, None], products, 0.0)
    return jax.ops.segment_sum(products, put_slot, num_segments=slot_total)


def all_sum(weight_term, bias_term):
    devices = lax.axis_size(("row", "col"))
    rows, width = weight_term.shape
    packed = jnp.concatenate([weight_term, bias_term[None, :]], axis=0)
    chunk = -(-(rows + 1) // devices)
    packed = jnp.pad(packed, ((0, chunk * devices - rows - 1), (0, 0)))
    parts = lax.all_to_all(
        packed.reshape(devices, chunk, width), ("row", "col"), 0, 0, tiled=True
    )
    owned = jnp.sum(parts, axis=0)
    spread = lax.all_to_all(
        jnp.broadcast_to(owned[None], (devices, chunk, width)), ("row", "col"), 0, 0, tiled=True
    ).reshape(devices * chunk, width)
    return spread[:rows], spread[rows]


def body(
    features,
    weight,
    layer_bias,
    adj_tiles,
    tile_source,
    tile_target,
    tile_count,
    fetch_list,
    deliver_list,
    cotangent,
):
    row_devices = lax.axis_size("row")
    col_devices = lax.axis_size("col")
    node_rows, feat_width = features.shape
    tile_side = adj_tiles.shape[1]
    own_blocks = node_rows // tile_side
    fetch_cap = fetch_list.shape[1]
    deliver_cap = deliver_list.shape[1]
    block_cells = tile_side * feat_width
    live_count = tile_count[0]
    projected = jnp.dot(features, weight, preferred_element_type=jnp.float32).astype(jnp.bfloat16)
    column = lax.all_gather(projected, "row", axis=0, tiled=True)
    source_operand = column.reshape(row_devices * own_blocks, tile_side, feat_width)
    global_ids = (
        jnp.arange(row_devices, dtype=jnp.int32)[:, None] * own_blocks + jnp.maximum(fetch_list, 0)
    ).reshape(-1)
    take_src = global_ids[tile_source]
    row_sums = tile_sums(
        adj_tiles,
        source_operand,
        take_src,
        tile_target,
        live_count,
        col_devices * deliver_cap,
        False,
    )
    outgoing_rows = row_sums.astype(jnp.bfloat16).reshape(col_devices, deliver_cap, block_cells)
    incoming = lax.all_to_all(outgoing_rows, "col", split_axis=0, concat_axis=0, tiled=True)
    deliver_hot = (
        deliver_list.reshape(-1)[None, :] == jnp.arange(own_blocks, dtype=jnp.int32)[:, None]
    ).astype(jnp.bfloat16)
    aggregated = jnp.dot(
        deliver_hot,
        incoming.reshape(col_devices * deliver_cap, block_cells),
        preferred_element_type=jnp.float32,
    )
    pre_act = aggregated.reshape(node_rows, feat_width) + layer_bias
    layer_out = jax.nn.silu(pre_act).astype(jnp.bfloat16)
    slopes = cotangent.astype(jnp.float32) * silu_grad(pre_act)
    bias_term = jnp.sum(slopes, axis=0)
    slope_blocks = slopes.astype(jnp.bfloat16).reshape(own_blocks, tile_side, feat_width)
    wanted_rows = slope_blocks[jnp.maximum(deliver_list, 0).reshape(-1)].reshape(
        col_devices, deliver_cap, tile_side, feat_width
    )
    row_values = lax.all_to_all(
        wanted_rows, "col", split_axis=0, concat_axis=0, tiled=True
    ).reshape(col_devices * deliver_cap, tile_side, feat_width)
    src_sums = tile_sums(
        adj_tiles, row_values, tile_target, tile_source, live_count, row_devices * fetch_cap, True
    )
    rounded = src_sums.astype(jnp.bfloat16).reshape(row_devices * fetch_cap, block_cells)
    valid_slots = fetch_list.reshape(-1) >= 0
    onehot = (
        (global_ids[None, :] == jnp.arange(row_devices * own_blocks, dtype=jnp.int32)[:, None])
        & valid_slots[None, :]
    ).astype(jnp.bfloat16)
    dense_rows = jnp.dot(onehot, rounded, preferred_element_type=jnp.float32)
    owned_sums = lax.psum_scatter(
        dense_rows.astype(jnp.bfloat16), "row", scatter_dimension=0, tiled=True
    ).astype(jnp.float32)
    grad_proj = owned_sums.reshape(node_rows, feat_width).astype(jnp.bfloat16)
    grad_features = jnp.dot(grad_proj, weight.T, preferred_element_type=jnp.float32).astype(
        jnp.bfloat16
    )
    weight_term = lax.dot_general(
        features, grad_proj, (((0,), (0,)), ((), ())), preferred_element_type=jnp.float32
    )
    grad_weight, grad_bias = all_sum(weight_term, bias_term)
    grad_scale = 1.0 / math.sqrt(node_rows * row_devices * col_devices)
    return (layer_out, grad_features, grad_weight * grad_scale, grad_bias * grad_scale)


def solution(mesh):
    return jax.shard_map(
        body,
        mesh=mesh,
        in_specs=(
            P(("row", "col"), None),
            P(),
            P(),
            P(("row", "col"), None, None),
            P(("row", "col")),
            P(("row", "col")),
            P(("row", "col")),
            P(("row", "col"), None),
            P(("row", "col"), None),
            P(("row", "col"), None),
        ),
        out_specs=(P(("row", "col"), None), P(("row", "col"), None), P(), P()),
        check_vma=False,
    )
```

```python
import math

import jax
import jax.numpy as jnp
from jax import lax
from jax.sharding import PartitionSpec as P


def silu_grad(values):
    logistic = jax.nn.sigmoid(values)
    return logistic * (1.0 + values * (1.0 - logistic))


def tile_sums(adj_tiles, operand, take_slot, put_slot, live_count, slot_total, transpose):
    pattern = "kji,kjf->kif" if transpose else "kij,kjf->kif"
    tile_total = adj_tiles.shape[0]
    live_mask = jnp.arange(tile_total, dtype=jnp.int32) < live_count
    products = jnp.einsum(
        pattern, adj_tiles, operand[take_slot], preferred_element_type=jnp.float32
    )
    products = jnp.where(live_mask[:, None, None], products, 0.0)
    return jax.ops.segment_sum(products, put_slot, num_segments=slot_total)


def all_sum(weight_term, bias_term):
    devices = lax.axis_size(("row", "col"))
    rows, width = weight_term.shape
    packed = jnp.concatenate([weight_term, bias_term[None, :]], axis=0)
    chunk = -(-(rows + 1) // devices)
    packed = jnp.pad(packed, ((0, chunk * devices - rows - 1), (0, 0)))
    parts = lax.all_to_all(
        packed.reshape(devices, chunk, width), ("row", "col"), 0, 0, tiled=True
    )
    owned = jnp.sum(parts, axis=0)
    spread = lax.all_to_all(
        jnp.broadcast_to(owned[None], (devices, chunk, width)), ("row", "col"), 0, 0, tiled=True
    ).reshape(devices * chunk, width)
    return spread[:rows], spread[rows]


def body(
    features,
    weight,
    layer_bias,
    adj_tiles,
    tile_source,
    tile_target,
    tile_count,
    fetch_list,
    deliver_list,
    cotangent,
):
    row_devices = lax.axis_size("row")
    col_devices = lax.axis_size("col")
    node_rows, feat_width = features.shape
    tile_side = adj_tiles.shape[1]
    own_blocks = node_rows // tile_side
    fetch_cap = fetch_list.shape[1]
    deliver_cap = deliver_list.shape[1]
    block_cells = tile_side * feat_width
    live_count = tile_count[0]
    projected = jnp.dot(features, weight, preferred_element_type=jnp.float32).astype(jnp.bfloat16)
    column = lax.all_gather(projected, "row", axis=0, tiled=True)
    source_operand = column.reshape(row_devices * own_blocks, tile_side, feat_width)
    global_ids = (
        jnp.arange(row_devices, dtype=jnp.int32)[:, None] * own_blocks + jnp.maximum(fetch_list, 0)
    ).reshape(-1)
    take_src = global_ids[tile_source]
    row_sums = tile_sums(
        adj_tiles,
        source_operand,
        take_src,
        tile_target,
        live_count,
        col_devices * deliver_cap,
        False,
    )
    outgoing_rows = row_sums.astype(jnp.bfloat16).reshape(
        col_devices, deliver_cap, tile_side, feat_width
    )
    incoming = lax.all_to_all(outgoing_rows, "col", split_axis=0, concat_axis=0, tiled=True)
    deliver_hot = (
        deliver_list.reshape(-1)[None, :] == jnp.arange(own_blocks, dtype=jnp.int32)[:, None]
    ).astype(jnp.bfloat16)
    aggregated = jnp.dot(
        deliver_hot,
        incoming.reshape(col_devices * deliver_cap, block_cells),
        preferred_element_type=jnp.float32,
    )
    pre_act = aggregated.reshape(node_rows, feat_width) + layer_bias
    layer_out = jax.nn.silu(pre_act).astype(jnp.bfloat16)
    slopes = cotangent.astype(jnp.float32) * silu_grad(pre_act)
    bias_term = jnp.sum(slopes, axis=0)
    slope_blocks = slopes.astype(jnp.bfloat16).reshape(own_blocks, tile_side, feat_width)
    wanted_rows = slope_blocks[jnp.maximum(deliver_list, 0).reshape(-1)].reshape(
        col_devices, deliver_cap, tile_side, feat_width
    )
    row_values = lax.all_to_all(
        wanted_rows, "col", split_axis=0, concat_axis=0, tiled=True
    ).reshape(col_devices * deliver_cap, tile_side, feat_width)
    src_sums = tile_sums(
        adj_tiles, row_values, tile_target, tile_source, live_count, row_devices * fetch_cap, True
    )
    rounded = src_sums.astype(jnp.bfloat16).reshape(row_devices * fetch_cap, block_cells)
    valid_slots = fetch_list.reshape(-1) >= 0
    onehot = (
        (global_ids[None, :] == jnp.arange(row_devices * own_blocks, dtype=jnp.int32)[:, None])
        & valid_slots[None, :]
    ).astype(jnp.bfloat16)
    dense_rows = jnp.dot(onehot, rounded, preferred_element_type=jnp.float32)
    owned_sums = lax.psum_scatter(
        dense_rows.astype(jnp.bfloat16), "row", scatter_dimension=0, tiled=True
    ).astype(jnp.float32)
    grad_proj = owned_sums.reshape(node_rows, feat_width).astype(jnp.bfloat16)
    grad_features = jnp.dot(grad_proj, weight.T, preferred_element_type=jnp.float32).astype(
        jnp.bfloat16
    )
    weight_term = lax.dot_general(
        features, grad_proj, (((0,), (0,)), ((), ())), preferred_element_type=jnp.float32
    )
    grad_weight, grad_bias = all_sum(weight_term, bias_term)
    grad_scale = 1.0 / math.sqrt(node_rows * row_devices * col_devices)
    return (layer_out, grad_features, grad_weight * grad_scale, grad_bias * grad_scale)


def solution(mesh):
    return jax.shard_map(
        body,
        mesh=mesh,
        in_specs=(
            P(("row", "col"), None),
            P(),
            P(),
            P(("row", "col"), None, None),
            P(("row", "col")),
            P(("row", "col")),
            P(("row", "col")),
            P(("row", "col"), None),
            P(("row", "col"), None),
            P(("row", "col"), None),
        ),
        out_specs=(P(("row", "col"), None), P(("row", "col"), None), P(), P()),
        check_vma=False,
    )
```

```python
import functools
import math

import jax
import jax.numpy as jnp
from jax import lax
from jax.experimental import pallas as pl
from jax.experimental.pallas import tpu as pltpu
from jax.sharding import PartitionSpec as P


def silu_grad(values):
    logistic = jax.nn.sigmoid(values)
    return logistic * (1.0 + values * (1.0 - logistic))


def tile_kernel(take_ref, put_ref, count_ref, adj_ref, operand_ref, out_ref, acc_ref, *, transpose):
    acc_ref[...] = jnp.zeros_like(acc_ref)

    def step(k, carry):
        tile = adj_ref[k]
        picked = operand_ref[take_ref[k]]
        if transpose:
            product = lax.dot_general(
                tile, picked, (((0,), (0,)), ((), ())), preferred_element_type=jnp.float32
            )
        else:
            product = jnp.dot(tile, picked, preferred_element_type=jnp.float32)
        slot = put_ref[k]
        acc_ref[slot] = acc_ref[slot] + product
        return carry

    lax.fori_loop(0, count_ref[0], step, 0)
    out_ref[...] = acc_ref[...].astype(out_ref.dtype)


def tile_sums(adj_tiles, operand, take_slot, put_slot, live_count, slot_total, transpose):
    tile_side = adj_tiles.shape[1]
    width = operand.shape[-1]
    smem = pl.BlockSpec(memory_space=pltpu.SMEM)
    vmem = pl.BlockSpec(memory_space=pltpu.VMEM)
    flops = 2 * adj_tiles.shape[0] * tile_side * tile_side * width
    moved = (adj_tiles.size + operand.size + slot_total * tile_side * width) * 2
    return pl.pallas_call(
        functools.partial(tile_kernel, transpose=transpose),
        out_shape=jax.ShapeDtypeStruct((slot_total, tile_side, width), jnp.bfloat16),
        in_specs=[smem, smem, smem, vmem, vmem],
        out_specs=vmem,
        scratch_shapes=[pltpu.VMEM((slot_total, tile_side, width), jnp.float32)],
        compiler_params=pltpu.CompilerParams(vmem_limit_bytes=56 * 1024 * 1024),
        cost_estimate=pl.CostEstimate(flops=flops, bytes_accessed=moved, transcendentals=0),
    )(
        take_slot.astype(jnp.int32),
        put_slot.astype(jnp.int32),
        jnp.reshape(live_count, (1,)).astype(jnp.int32),
        adj_tiles,
        operand,
    )


def all_sum(weight_term, bias_term):
    devices = lax.axis_size(("row", "col"))
    rows, width = weight_term.shape
    packed = jnp.concatenate([weight_term, bias_term[None, :]], axis=0)
    chunk = -(-(rows + 1) // devices)
    packed = jnp.pad(packed, ((0, chunk * devices - rows - 1), (0, 0)))
    parts = lax.all_to_all(
        packed.reshape(devices, chunk, width), ("row", "col"), 0, 0, tiled=True
    )
    owned = jnp.sum(parts, axis=0)
    spread = lax.all_to_all(
        jnp.broadcast_to(owned[None], (devices, chunk, width)), ("row", "col"), 0, 0, tiled=True
    ).reshape(devices * chunk, width)
    return spread[:rows], spread[rows]


def body(
    features,
    weight,
    layer_bias,
    adj_tiles,
    tile_source,
    tile_target,
    tile_count,
    fetch_list,
    deliver_list,
    cotangent,
):
    row_devices = lax.axis_size("row")
    col_devices = lax.axis_size("col")
    node_rows, feat_width = features.shape
    tile_side = adj_tiles.shape[1]
    own_blocks = node_rows // tile_side
    fetch_cap = fetch_list.shape[1]
    deliver_cap = deliver_list.shape[1]
    block_cells = tile_side * feat_width
    live_count = tile_count[0]
    projected = jnp.dot(features, weight, preferred_element_type=jnp.float32).astype(jnp.bfloat16)
    column = lax.all_gather(projected, "row", axis=0, tiled=True)
    source_operand = column.reshape(row_devices * own_blocks, tile_side, feat_width)
    global_ids = (
        jnp.arange(row_devices, dtype=jnp.int32)[:, None] * own_blocks + jnp.maximum(fetch_list, 0)
    ).reshape(-1)
    take_src = global_ids[tile_source]
    row_sums = tile_sums(
        adj_tiles,
        source_operand,
        take_src,
        tile_target,
        live_count,
        col_devices * deliver_cap,
        False,
    )
    outgoing_rows = row_sums.reshape(
        col_devices, deliver_cap, tile_side, feat_width
    )
    incoming = lax.all_to_all(outgoing_rows, "col", split_axis=0, concat_axis=0, tiled=True)
    deliver_hot = (
        deliver_list.reshape(-1)[None, :] == jnp.arange(own_blocks, dtype=jnp.int32)[:, None]
    ).astype(jnp.bfloat16)
    aggregated = jnp.dot(
        deliver_hot,
        incoming.reshape(col_devices * deliver_cap, block_cells),
        preferred_element_type=jnp.float32,
    )
    pre_act = aggregated.reshape(node_rows, feat_width) + layer_bias
    layer_out = jax.nn.silu(pre_act).astype(jnp.bfloat16)
    slopes = cotangent.astype(jnp.float32) * silu_grad(pre_act)
    bias_term = jnp.sum(slopes, axis=0)
    slope_blocks = slopes.astype(jnp.bfloat16).reshape(own_blocks, tile_side, feat_width)
    wanted_rows = slope_blocks[jnp.maximum(deliver_list, 0).reshape(-1)].reshape(
        col_devices, deliver_cap, tile_side, feat_width
    )
    row_values = lax.all_to_all(
        wanted_rows, "col", split_axis=0, concat_axis=0, tiled=True
    ).reshape(col_devices * deliver_cap, tile_side, feat_width)
    src_sums = tile_sums(
        adj_tiles, row_values, tile_target, tile_source, live_count, row_devices * fetch_cap, True
    )
    rounded = src_sums.reshape(row_devices * fetch_cap, block_cells)
    valid_slots = fetch_list.reshape(-1) >= 0
    onehot = (
        (global_ids[None, :] == jnp.arange(row_devices * own_blocks, dtype=jnp.int32)[:, None])
        & valid_slots[None, :]
    ).astype(jnp.bfloat16)
    dense_rows = jnp.dot(onehot, rounded, preferred_element_type=jnp.float32)
    owned_sums = lax.psum_scatter(
        dense_rows.astype(jnp.bfloat16), "row", scatter_dimension=0, tiled=True
    ).astype(jnp.float32)
    grad_proj = owned_sums.reshape(node_rows, feat_width).astype(jnp.bfloat16)
    grad_features = jnp.dot(grad_proj, weight.T, preferred_element_type=jnp.float32).astype(
        jnp.bfloat16
    )
    weight_term = lax.dot_general(
        features, grad_proj, (((0,), (0,)), ((), ())), preferred_element_type=jnp.float32
    )
    grad_weight, grad_bias = all_sum(weight_term, bias_term)
    grad_scale = 1.0 / math.sqrt(node_rows * row_devices * col_devices)
    return (layer_out, grad_features, grad_weight * grad_scale, grad_bias * grad_scale)


def solution(mesh):
    return jax.shard_map(
        body,
        mesh=mesh,
        in_specs=(
            P(("row", "col"), None),
            P(),
            P(),
            P(("row", "col"), None, None),
            P(("row", "col")),
            P(("row", "col")),
            P(("row", "col")),
            P(("row", "col"), None),
            P(("row", "col"), None),
            P(("row", "col"), None),
        ),
        out_specs=(P(("row", "col"), None), P(("row", "col"), None), P(), P()),
        check_vma=False,
    )
```

```python
import functools
import math

import jax
import jax.numpy as jnp
from jax import lax
from jax.experimental import pallas as pl
from jax.experimental.pallas import tpu as pltpu
from jax.sharding import PartitionSpec as P


def silu_grad(values):
    logistic = jax.nn.sigmoid(values)
    return logistic * (1.0 + values * (1.0 - logistic))


def tile_kernel(take_ref, put_ref, count_ref, adj_ref, operand_ref, out_ref, acc_ref, *, transpose):
    acc_ref[...] = jnp.zeros_like(acc_ref)

    def step(k, carry):
        tile = adj_ref[k]
        picked = operand_ref[take_ref[k]]
        if transpose:
            product = lax.dot_general(
                tile, picked, (((0,), (0,)), ((), ())), preferred_element_type=jnp.float32
            )
        else:
            product = jnp.dot(tile, picked, preferred_element_type=jnp.float32)
        slot = put_ref[k]
        acc_ref[slot] = acc_ref[slot] + product
        return carry

    lax.fori_loop(0, count_ref[0], step, 0)
    out_ref[...] = acc_ref[...].astype(out_ref.dtype)


def tile_sums(adj_tiles, operand, take_slot, put_slot, live_count, slot_total, transpose):
    tile_side = adj_tiles.shape[1]
    width = operand.shape[-1]
    smem = pl.BlockSpec(memory_space=pltpu.SMEM)
    vmem = pl.BlockSpec(memory_space=pltpu.VMEM)
    flops = 2 * adj_tiles.shape[0] * tile_side * tile_side * width
    moved = (adj_tiles.size + operand.size + slot_total * tile_side * width) * 2
    return pl.pallas_call(
        functools.partial(tile_kernel, transpose=transpose),
        out_shape=jax.ShapeDtypeStruct((slot_total, tile_side, width), jnp.bfloat16),
        in_specs=[smem, smem, smem, vmem, vmem],
        out_specs=vmem,
        scratch_shapes=[pltpu.VMEM((slot_total, tile_side, width), jnp.float32)],
        compiler_params=pltpu.CompilerParams(vmem_limit_bytes=56 * 1024 * 1024),
        cost_estimate=pl.CostEstimate(flops=flops, bytes_accessed=moved, transcendentals=0),
    )(
        take_slot.astype(jnp.int32),
        put_slot.astype(jnp.int32),
        jnp.reshape(live_count, (1,)).astype(jnp.int32),
        adj_tiles,
        operand,
    )


def all_sum(weight_term, bias_term):
    devices = lax.axis_size(("row", "col"))
    rows, width = weight_term.shape
    packed = jnp.concatenate([weight_term, bias_term[None, :]], axis=0)
    chunk = -(-(rows + 1) // devices)
    packed = jnp.pad(packed, ((0, chunk * devices - rows - 1), (0, 0)))
    parts = lax.all_to_all(
        packed.reshape(devices, chunk, width), ("row", "col"), 0, 0, tiled=True
    )
    owned = jnp.sum(parts, axis=0)
    spread = lax.all_to_all(
        jnp.broadcast_to(owned[None], (devices, chunk, width)), ("row", "col"), 0, 0, tiled=True
    ).reshape(devices * chunk, width)
    return spread[:rows], spread[rows]


def body(
    features,
    weight,
    layer_bias,
    adj_tiles,
    tile_source,
    tile_target,
    tile_count,
    fetch_list,
    deliver_list,
    cotangent,
):
    row_devices = lax.axis_size("row")
    col_devices = lax.axis_size("col")
    node_rows, feat_width = features.shape
    tile_side = adj_tiles.shape[1]
    own_blocks = node_rows // tile_side
    fetch_cap = fetch_list.shape[1]
    deliver_cap = deliver_list.shape[1]
    block_cells = tile_side * feat_width
    live_count = tile_count[0]
    column_features = lax.all_gather(features, "row", axis=0, tiled=True)
    column = jnp.dot(column_features, weight, preferred_element_type=jnp.float32).astype(
        jnp.bfloat16
    )
    source_operand = column.reshape(row_devices * own_blocks, tile_side, feat_width)
    global_ids = (
        jnp.arange(row_devices, dtype=jnp.int32)[:, None] * own_blocks + jnp.maximum(fetch_list, 0)
    ).reshape(-1)
    take_src = global_ids[tile_source]
    row_sums = tile_sums(
        adj_tiles,
        source_operand,
        take_src,
        tile_target,
        live_count,
        col_devices * deliver_cap,
        False,
    )
    outgoing_rows = row_sums.reshape(
        col_devices, deliver_cap, tile_side, feat_width
    )
    incoming = lax.all_to_all(outgoing_rows, "col", split_axis=0, concat_axis=0, tiled=True)
    deliver_hot = (
        deliver_list.reshape(-1)[None, :] == jnp.arange(own_blocks, dtype=jnp.int32)[:, None]
    ).astype(jnp.bfloat16)
    aggregated = jnp.dot(
        deliver_hot,
        incoming.reshape(col_devices * deliver_cap, block_cells),
        preferred_element_type=jnp.float32,
    )
    pre_act = aggregated.reshape(node_rows, feat_width) + layer_bias
    layer_out = jax.nn.silu(pre_act).astype(jnp.bfloat16)
    slopes = cotangent.astype(jnp.float32) * silu_grad(pre_act)
    bias_term = jnp.sum(slopes, axis=0)
    slope_blocks = slopes.astype(jnp.bfloat16).reshape(own_blocks, tile_side, feat_width)
    wanted_rows = slope_blocks[jnp.maximum(deliver_list, 0).reshape(-1)].reshape(
        col_devices, deliver_cap, tile_side, feat_width
    )
    row_values = lax.all_to_all(
        wanted_rows, "col", split_axis=0, concat_axis=0, tiled=True
    ).reshape(col_devices * deliver_cap, tile_side, feat_width)
    src_sums = tile_sums(
        adj_tiles, row_values, tile_target, tile_source, live_count, row_devices * fetch_cap, True
    )
    rounded = src_sums.reshape(row_devices * fetch_cap, block_cells)
    valid_slots = fetch_list.reshape(-1) >= 0
    onehot = (
        (global_ids[None, :] == jnp.arange(row_devices * own_blocks, dtype=jnp.int32)[:, None])
        & valid_slots[None, :]
    ).astype(jnp.bfloat16)
    dense_rows = jnp.dot(onehot, rounded, preferred_element_type=jnp.float32).astype(jnp.bfloat16)
    weight_term = lax.dot_general(
        column_features,
        dense_rows.reshape(row_devices * node_rows, feat_width),
        (((0,), (0,)), ((), ())),
        preferred_element_type=jnp.float32,
    )
    grad_weight, grad_bias = all_sum(weight_term, bias_term)
    owned_sums = lax.psum_scatter(
        dense_rows, "row", scatter_dimension=0, tiled=True
    ).astype(jnp.float32)
    grad_proj = owned_sums.reshape(node_rows, feat_width).astype(jnp.bfloat16)
    grad_features = jnp.dot(grad_proj, weight.T, preferred_element_type=jnp.float32).astype(
        jnp.bfloat16
    )
    grad_scale = 1.0 / math.sqrt(node_rows * row_devices * col_devices)
    return (layer_out, grad_features, grad_weight * grad_scale, grad_bias * grad_scale)


def solution(mesh):
    return jax.shard_map(
        body,
        mesh=mesh,
        in_specs=(
            P(("row", "col"), None),
            P(),
            P(),
            P(("row", "col"), None, None),
            P(("row", "col")),
            P(("row", "col")),
            P(("row", "col")),
            P(("row", "col"), None),
            P(("row", "col"), None),
            P(("row", "col"), None),
        ),
        out_specs=(P(("row", "col"), None), P(("row", "col"), None), P(), P()),
        check_vma=False,
    )
```

```python
import functools
import math

import jax
import jax.numpy as jnp
from jax import lax
from jax.experimental import pallas as pl
from jax.experimental.pallas import tpu as pltpu
from jax.sharding import PartitionSpec as P


def silu_grad(values):
    logistic = jax.nn.sigmoid(values)
    return logistic * (1.0 + values * (1.0 - logistic))


def tile_kernel(take_ref, put_ref, count_ref, adj_ref, operand_ref, out_ref, acc_ref, *, transpose):
    acc_ref[...] = jnp.zeros_like(acc_ref)

    def step(k, carry):
        tile = adj_ref[k]
        picked = operand_ref[take_ref[k]]
        if transpose:
            product = lax.dot_general(
                tile, picked, (((0,), (0,)), ((), ())), preferred_element_type=jnp.float32
            )
        else:
            product = jnp.dot(tile, picked, preferred_element_type=jnp.float32)
        slot = put_ref[k]
        acc_ref[slot] = acc_ref[slot] + product
        return carry

    lax.fori_loop(0, count_ref[0], step, 0)
    out_ref[...] = acc_ref[...].astype(out_ref.dtype)


def tile_sums(adj_tiles, operand, take_slot, put_slot, live_count, slot_total, transpose):
    tile_side = adj_tiles.shape[1]
    width = operand.shape[-1]
    smem = pl.BlockSpec(memory_space=pltpu.SMEM)
    vmem = pl.BlockSpec(memory_space=pltpu.VMEM)
    flops = 2 * adj_tiles.shape[0] * tile_side * tile_side * width
    moved = (adj_tiles.size + operand.size + slot_total * tile_side * width) * 2
    return pl.pallas_call(
        functools.partial(tile_kernel, transpose=transpose),
        out_shape=jax.ShapeDtypeStruct((slot_total, tile_side, width), jnp.bfloat16),
        in_specs=[smem, smem, smem, vmem, vmem],
        out_specs=vmem,
        scratch_shapes=[pltpu.VMEM((slot_total, tile_side, width), jnp.float32)],
        compiler_params=pltpu.CompilerParams(vmem_limit_bytes=56 * 1024 * 1024),
        cost_estimate=pl.CostEstimate(flops=flops, bytes_accessed=moved, transcendentals=0),
    )(
        take_slot.astype(jnp.int32),
        put_slot.astype(jnp.int32),
        jnp.reshape(live_count, (1,)).astype(jnp.int32),
        adj_tiles,
        operand,
    )


def all_sum(weight_term, bias_term):
    devices = lax.axis_size(("row", "col"))
    rows, width = weight_term.shape
    packed = jnp.concatenate([weight_term, bias_term[None, :]], axis=0)
    chunk = -(-(rows + 1) // devices)
    packed = jnp.pad(packed, ((0, chunk * devices - rows - 1), (0, 0)))
    parts = lax.all_to_all(
        packed.reshape(devices, chunk, width), ("row", "col"), 0, 0, tiled=True
    )
    owned = jnp.sum(parts, axis=0)
    spread = lax.all_to_all(
        jnp.broadcast_to(owned[None], (devices, chunk, width)), ("row", "col"), 0, 0, tiled=True
    ).reshape(devices * chunk, width)
    return spread[:rows], spread[rows]


def body(
    features,
    weight,
    layer_bias,
    adj_tiles,
    tile_source,
    tile_target,
    tile_count,
    fetch_list,
    deliver_list,
    cotangent,
):
    row_devices = lax.axis_size("row")
    col_devices = lax.axis_size("col")
    node_rows, feat_width = features.shape
    tile_side = adj_tiles.shape[1]
    own_blocks = node_rows // tile_side
    fetch_cap = fetch_list.shape[1]
    deliver_cap = deliver_list.shape[1]
    block_cells = tile_side * feat_width
    live_count = tile_count[0]
    column_features = lax.all_to_all(
        jnp.broadcast_to(features[None], (row_devices, node_rows, feat_width)),
        "row",
        0,
        0,
        tiled=True,
    ).reshape(row_devices * node_rows, feat_width)
    column = jnp.dot(column_features, weight, preferred_element_type=jnp.float32).astype(
        jnp.bfloat16
    )
    source_operand = column.reshape(row_devices * own_blocks, tile_side, feat_width)
    global_ids = (
        jnp.arange(row_devices, dtype=jnp.int32)[:, None] * own_blocks + jnp.maximum(fetch_list, 0)
    ).reshape(-1)
    take_src = global_ids[tile_source]
    row_sums = tile_sums(
        adj_tiles,
        source_operand,
        take_src,
        tile_target,
        live_count,
        col_devices * deliver_cap,
        False,
    )
    outgoing_rows = row_sums.reshape(
        col_devices, deliver_cap, tile_side, feat_width
    )
    incoming = lax.all_to_all(outgoing_rows, "col", split_axis=0, concat_axis=0, tiled=True)
    deliver_hot = (
        deliver_list.reshape(-1)[None, :] == jnp.arange(own_blocks, dtype=jnp.int32)[:, None]
    ).astype(jnp.bfloat16)
    aggregated = jnp.dot(
        deliver_hot,
        incoming.reshape(col_devices * deliver_cap, block_cells),
        preferred_element_type=jnp.float32,
    )
    pre_act = aggregated.reshape(node_rows, feat_width) + layer_bias
    layer_out = jax.nn.silu(pre_act).astype(jnp.bfloat16)
    slopes = cotangent.astype(jnp.float32) * silu_grad(pre_act)
    bias_term = jnp.sum(slopes, axis=0)
    slope_blocks = slopes.astype(jnp.bfloat16).reshape(own_blocks, tile_side, feat_width)
    wanted_rows = slope_blocks[jnp.maximum(deliver_list, 0).reshape(-1)].reshape(
        col_devices, deliver_cap, tile_side, feat_width
    )
    row_values = lax.all_to_all(
        wanted_rows, "col", split_axis=0, concat_axis=0, tiled=True
    ).reshape(col_devices * deliver_cap, tile_side, feat_width)
    src_sums = tile_sums(
        adj_tiles, row_values, tile_target, tile_source, live_count, row_devices * fetch_cap, True
    )
    rounded = src_sums.reshape(row_devices * fetch_cap, block_cells)
    valid_slots = fetch_list.reshape(-1) >= 0
    onehot = (
        (global_ids[None, :] == jnp.arange(row_devices * own_blocks, dtype=jnp.int32)[:, None])
        & valid_slots[None, :]
    ).astype(jnp.bfloat16)
    dense_rows = jnp.dot(onehot, rounded, preferred_element_type=jnp.float32).astype(jnp.bfloat16)
    weight_term = lax.dot_general(
        column_features,
        dense_rows.reshape(row_devices * node_rows, feat_width),
        (((0,), (0,)), ((), ())),
        preferred_element_type=jnp.float32,
    )
    grad_weight, grad_bias = all_sum(weight_term, bias_term)
    owned_sums = jnp.sum(
        lax.all_to_all(
            dense_rows.reshape(row_devices, own_blocks, tile_side, feat_width),
            "row",
            0,
            0,
            tiled=True,
        ).astype(jnp.float32),
        axis=0,
    )
    grad_proj = owned_sums.reshape(node_rows, feat_width).astype(jnp.bfloat16)
    grad_features = jnp.dot(grad_proj, weight.T, preferred_element_type=jnp.float32).astype(
        jnp.bfloat16
    )
    grad_scale = 1.0 / math.sqrt(node_rows * row_devices * col_devices)
    return (layer_out, grad_features, grad_weight * grad_scale, grad_bias * grad_scale)


def solution(mesh):
    return jax.shard_map(
        body,
        mesh=mesh,
        in_specs=(
            P(("row", "col"), None),
            P(),
            P(),
            P(("row", "col"), None, None),
            P(("row", "col")),
            P(("row", "col")),
            P(("row", "col")),
            P(("row", "col"), None),
            P(("row", "col"), None),
            P(("row", "col"), None),
        ),
        out_specs=(P(("row", "col"), None), P(("row", "col"), None), P(), P()),
        check_vma=False,
    )
```

```python
import functools
import math

import jax
import jax.numpy as jnp
from jax import lax
from jax.experimental import pallas as pl
from jax.experimental.pallas import tpu as pltpu
from jax.sharding import PartitionSpec as P


def silu_grad(values):
    logistic = jax.nn.sigmoid(values)
    return logistic * (1.0 + values * (1.0 - logistic))


def tile_kernel(take_ref, put_ref, count_ref, adj_ref, operand_ref, out_ref, acc_ref, *, transpose):
    acc_ref[...] = jnp.zeros_like(acc_ref)

    def step(k, carry):
        tile = adj_ref[k]
        picked = operand_ref[take_ref[k]]
        if transpose:
            product = lax.dot_general(
                tile, picked, (((0,), (0,)), ((), ())), preferred_element_type=jnp.float32
            )
        else:
            product = jnp.dot(tile, picked, preferred_element_type=jnp.float32)
        slot = put_ref[k]
        acc_ref[slot] = acc_ref[slot] + product
        return carry

    lax.fori_loop(0, count_ref[0], step, 0)
    out_ref[...] = acc_ref[...].astype(out_ref.dtype)


def tile_sums(adj_tiles, operand, take_slot, put_slot, live_count, slot_total, transpose):
    tile_side = adj_tiles.shape[1]
    width = operand.shape[-1]
    smem = pl.BlockSpec(memory_space=pltpu.SMEM)
    vmem = pl.BlockSpec(memory_space=pltpu.VMEM)
    flops = 2 * adj_tiles.shape[0] * tile_side * tile_side * width
    moved = (adj_tiles.size + operand.size + slot_total * tile_side * width) * 2
    return pl.pallas_call(
        functools.partial(tile_kernel, transpose=transpose),
        out_shape=jax.ShapeDtypeStruct((slot_total, tile_side, width), jnp.bfloat16),
        in_specs=[smem, smem, smem, vmem, vmem],
        out_specs=vmem,
        scratch_shapes=[pltpu.VMEM((slot_total, tile_side, width), jnp.float32)],
        compiler_params=pltpu.CompilerParams(vmem_limit_bytes=56 * 1024 * 1024),
        cost_estimate=pl.CostEstimate(flops=flops, bytes_accessed=moved, transcendentals=0),
    )(
        take_slot.astype(jnp.int32),
        put_slot.astype(jnp.int32),
        jnp.reshape(live_count, (1,)).astype(jnp.int32),
        adj_tiles,
        operand,
    )


def all_sum(weight_term, bias_term):
    devices = lax.axis_size(("row", "col"))
    rows, width = weight_term.shape
    packed = jnp.concatenate([weight_term, bias_term[None, :]], axis=0)
    chunk = -(-(rows + 1) // devices)
    packed = jnp.pad(packed, ((0, chunk * devices - rows - 1), (0, 0)))
    parts = lax.all_to_all(
        packed.reshape(devices, chunk, width), ("row", "col"), 0, 0, tiled=True
    )
    owned = jnp.sum(parts, axis=0)
    spread = lax.all_to_all(
        jnp.broadcast_to(owned[None], (devices, chunk, width)), ("row", "col"), 0, 0, tiled=True
    ).reshape(devices * chunk, width)
    return spread[:rows], spread[rows]


def body(
    features,
    weight,
    layer_bias,
    adj_tiles,
    tile_source,
    tile_target,
    tile_count,
    fetch_list,
    deliver_list,
    cotangent,
):
    row_devices = lax.axis_size("row")
    col_devices = lax.axis_size("col")
    node_rows, feat_width = features.shape
    tile_side = adj_tiles.shape[1]
    own_blocks = node_rows // tile_side
    fetch_cap = fetch_list.shape[1]
    deliver_cap = deliver_list.shape[1]
    block_cells = tile_side * feat_width
    live_count = tile_count[0]
    column_features = lax.all_gather(features, "row", axis=0, tiled=True)
    column = jnp.dot(column_features, weight, preferred_element_type=jnp.float32).astype(
        jnp.bfloat16
    )
    source_operand = column.reshape(row_devices * own_blocks, tile_side, feat_width)
    global_ids = (
        jnp.arange(row_devices, dtype=jnp.int32)[:, None] * own_blocks + jnp.maximum(fetch_list, 0)
    ).reshape(-1)
    take_src = global_ids[tile_source]
    row_sums = tile_sums(
        adj_tiles,
        source_operand,
        take_src,
        tile_target,
        live_count,
        col_devices * deliver_cap,
        False,
    )
    outgoing_rows = row_sums.reshape(
        col_devices, deliver_cap, tile_side, feat_width
    )
    incoming = lax.all_to_all(outgoing_rows, "col", split_axis=0, concat_axis=0, tiled=True)
    deliver_hot = (
        deliver_list.reshape(-1)[None, :] == jnp.arange(own_blocks, dtype=jnp.int32)[:, None]
    ).astype(jnp.bfloat16)
    aggregated = jnp.dot(
        deliver_hot,
        incoming.reshape(col_devices * deliver_cap, block_cells),
        preferred_element_type=jnp.float32,
    )
    pre_act = aggregated.reshape(node_rows, feat_width) + layer_bias
    layer_out = jax.nn.silu(pre_act).astype(jnp.bfloat16)
    slopes = cotangent.astype(jnp.float32) * silu_grad(pre_act)
    bias_term = jnp.sum(slopes, axis=0)
    slope_blocks = slopes.astype(jnp.bfloat16).reshape(own_blocks, tile_side, feat_width)
    wanted_rows = slope_blocks[jnp.maximum(deliver_list, 0).reshape(-1)].reshape(
        col_devices, deliver_cap, tile_side, feat_width
    )
    row_values = lax.all_to_all(
        wanted_rows, "col", split_axis=0, concat_axis=0, tiled=True
    ).reshape(col_devices * deliver_cap, tile_side, feat_width)
    src_sums = tile_sums(
        adj_tiles, row_values, tile_target, tile_source, live_count, row_devices * fetch_cap, True
    )
    rounded = src_sums.reshape(row_devices * fetch_cap, block_cells)
    valid_slots = fetch_list.reshape(-1) >= 0
    onehot = (
        (global_ids[None, :] == jnp.arange(row_devices * own_blocks, dtype=jnp.int32)[:, None])
        & valid_slots[None, :]
    ).astype(jnp.bfloat16)
    dense_rows = jnp.dot(onehot, rounded, preferred_element_type=jnp.float32).astype(jnp.bfloat16)
    slot_features = column_features.reshape(row_devices * own_blocks, tile_side, feat_width)[
        global_ids
    ]
    weight_term = lax.dot_general(
        slot_features.reshape(row_devices * fetch_cap * tile_side, feat_width),
        src_sums.reshape(row_devices * fetch_cap * tile_side, feat_width),
        (((0,), (0,)), ((), ())),
        preferred_element_type=jnp.float32,
    )
    grad_weight, grad_bias = all_sum(weight_term, bias_term)
    owned_sums = lax.psum_scatter(
        dense_rows, "row", scatter_dimension=0, tiled=True
    ).astype(jnp.float32)
    grad_proj = owned_sums.reshape(node_rows, feat_width).astype(jnp.bfloat16)
    grad_features = jnp.dot(grad_proj, weight.T, preferred_element_type=jnp.float32).astype(
        jnp.bfloat16
    )
    grad_scale = 1.0 / math.sqrt(node_rows * row_devices * col_devices)
    return (layer_out, grad_features, grad_weight * grad_scale, grad_bias * grad_scale)


def solution(mesh):
    return jax.shard_map(
        body,
        mesh=mesh,
        in_specs=(
            P(("row", "col"), None),
            P(),
            P(),
            P(("row", "col"), None, None),
            P(("row", "col")),
            P(("row", "col")),
            P(("row", "col")),
            P(("row", "col"), None),
            P(("row", "col"), None),
            P(("row", "col"), None),
        ),
        out_specs=(P(("row", "col"), None), P(("row", "col"), None), P(), P()),
        check_vma=False,
    )
```

```python
import functools
import math

import jax
import jax.numpy as jnp
from jax import lax
from jax.experimental import pallas as pl
from jax.experimental.pallas import tpu as pltpu
from jax.sharding import PartitionSpec as P


def silu_grad(values):
    logistic = jax.nn.sigmoid(values)
    return logistic * (1.0 + values * (1.0 - logistic))


def tile_kernel(take_ref, put_ref, count_ref, adj_ref, operand_ref, out_ref, acc_ref, *, transpose):
    acc_ref[...] = jnp.zeros_like(acc_ref)

    def step(k, carry):
        tile = adj_ref[k]
        picked = operand_ref[take_ref[k]]
        if transpose:
            product = lax.dot_general(
                tile, picked, (((0,), (0,)), ((), ())), preferred_element_type=jnp.float32
            )
        else:
            product = jnp.dot(tile, picked, preferred_element_type=jnp.float32)
        slot = put_ref[k]
        acc_ref[slot] = acc_ref[slot] + product
        return carry

    lax.fori_loop(0, count_ref[0], step, 0)
    out_ref[...] = acc_ref[...].astype(out_ref.dtype)


def tile_sums(adj_tiles, operand, take_slot, put_slot, live_count, slot_total, transpose):
    tile_side = adj_tiles.shape[1]
    width = operand.shape[-1]
    smem = pl.BlockSpec(memory_space=pltpu.SMEM)
    vmem = pl.BlockSpec(memory_space=pltpu.VMEM)
    flops = 2 * adj_tiles.shape[0] * tile_side * tile_side * width
    moved = (adj_tiles.size + operand.size + slot_total * tile_side * width) * 2
    return pl.pallas_call(
        functools.partial(tile_kernel, transpose=transpose),
        out_shape=jax.ShapeDtypeStruct((slot_total, tile_side, width), jnp.bfloat16),
        in_specs=[smem, smem, smem, vmem, vmem],
        out_specs=vmem,
        scratch_shapes=[pltpu.VMEM((slot_total, tile_side, width), jnp.float32)],
        compiler_params=pltpu.CompilerParams(vmem_limit_bytes=56 * 1024 * 1024),
        cost_estimate=pl.CostEstimate(flops=flops, bytes_accessed=moved, transcendentals=0),
    )(
        take_slot.astype(jnp.int32),
        put_slot.astype(jnp.int32),
        jnp.reshape(live_count, (1,)).astype(jnp.int32),
        adj_tiles,
        operand,
    )


def slot_add_kernel(put_ref, operand_ref, out_ref):
    out_ref[...] = jnp.zeros_like(out_ref)

    def step(s, carry):
        block = put_ref[s]
        out_ref[block] = out_ref[block] + operand_ref[s].astype(jnp.float32)
        return carry

    lax.fori_loop(0, operand_ref.shape[0], step, 0)


def slot_add(operand, put_block, block_total):
    tile_side, width = operand.shape[1:]
    smem = pl.BlockSpec(memory_space=pltpu.SMEM)
    vmem = pl.BlockSpec(memory_space=pltpu.VMEM)
    summed = pl.pallas_call(
        slot_add_kernel,
        out_shape=jax.ShapeDtypeStruct((block_total + 1, tile_side, width), jnp.float32),
        in_specs=[smem, vmem],
        out_specs=vmem,
        compiler_params=pltpu.CompilerParams(vmem_limit_bytes=32 * 1024 * 1024),
        cost_estimate=pl.CostEstimate(
            flops=operand.size,
            bytes_accessed=operand.size * 2 + (block_total + 1) * tile_side * width * 4,
            transcendentals=0,
        ),
    )(put_block.astype(jnp.int32), operand)
    return summed[:block_total]


def all_sum(weight_term, bias_term):
    devices = lax.axis_size(("row", "col"))
    rows, width = weight_term.shape
    packed = jnp.concatenate([weight_term, bias_term[None, :]], axis=0)
    chunk = -(-(rows + 1) // devices)
    packed = jnp.pad(packed, ((0, chunk * devices - rows - 1), (0, 0)))
    parts = lax.all_to_all(
        packed.reshape(devices, chunk, width), ("row", "col"), 0, 0, tiled=True
    )
    owned = jnp.sum(parts, axis=0)
    spread = lax.all_to_all(
        jnp.broadcast_to(owned[None], (devices, chunk, width)), ("row", "col"), 0, 0, tiled=True
    ).reshape(devices * chunk, width)
    return spread[:rows], spread[rows]


def body(
    features,
    weight,
    layer_bias,
    adj_tiles,
    tile_source,
    tile_target,
    tile_count,
    fetch_list,
    deliver_list,
    cotangent,
):
    row_devices = lax.axis_size("row")
    col_devices = lax.axis_size("col")
    node_rows, feat_width = features.shape
    tile_side = adj_tiles.shape[1]
    own_blocks = node_rows // tile_side
    fetch_cap = fetch_list.shape[1]
    deliver_cap = deliver_list.shape[1]
    block_cells = tile_side * feat_width
    live_count = tile_count[0]
    column_features = lax.all_gather(features, "row", axis=0, tiled=True)
    column = jnp.dot(column_features, weight, preferred_element_type=jnp.float32).astype(
        jnp.bfloat16
    )
    source_operand = column.reshape(row_devices * own_blocks, tile_side, feat_width)
    global_ids = (
        jnp.arange(row_devices, dtype=jnp.int32)[:, None] * own_blocks + jnp.maximum(fetch_list, 0)
    ).reshape(-1)
    take_src = global_ids[tile_source]
    row_sums = tile_sums(
        adj_tiles,
        source_operand,
        take_src,
        tile_target,
        live_count,
        col_devices * deliver_cap,
        False,
    )
    outgoing_rows = row_sums.reshape(
        col_devices, deliver_cap, tile_side, feat_width
    )
    incoming = lax.all_to_all(outgoing_rows, "col", split_axis=0, concat_axis=0, tiled=True)
    deliver_flat = deliver_list.reshape(-1)
    aggregated = slot_add(
        incoming.reshape(col_devices * deliver_cap, tile_side, feat_width),
        jnp.where(deliver_flat >= 0, deliver_flat, own_blocks),
        own_blocks,
    )
    pre_act = aggregated.reshape(node_rows, feat_width) + layer_bias
    layer_out = jax.nn.silu(pre_act).astype(jnp.bfloat16)
    slopes = cotangent.astype(jnp.float32) * silu_grad(pre_act)
    bias_term = jnp.sum(slopes, axis=0)
    slope_blocks = slopes.astype(jnp.bfloat16).reshape(own_blocks, tile_side, feat_width)
    wanted_rows = slope_blocks[jnp.maximum(deliver_list, 0).reshape(-1)].reshape(
        col_devices, deliver_cap, tile_side, feat_width
    )
    row_values = lax.all_to_all(
        wanted_rows, "col", split_axis=0, concat_axis=0, tiled=True
    ).reshape(col_devices * deliver_cap, tile_side, feat_width)
    src_sums = tile_sums(
        adj_tiles, row_values, tile_target, tile_source, live_count, row_devices * fetch_cap, True
    )
    rounded = src_sums.reshape(row_devices * fetch_cap, block_cells)
    valid_slots = fetch_list.reshape(-1) >= 0
    onehot = (
        (global_ids[None, :] == jnp.arange(row_devices * own_blocks, dtype=jnp.int32)[:, None])
        & valid_slots[None, :]
    ).astype(jnp.bfloat16)
    dense_rows = jnp.dot(onehot, rounded, preferred_element_type=jnp.float32).astype(jnp.bfloat16)
    slot_features = column_features.reshape(row_devices * own_blocks, tile_side, feat_width)[
        global_ids
    ]
    weight_term = lax.dot_general(
        slot_features.reshape(row_devices * fetch_cap * tile_side, feat_width),
        src_sums.reshape(row_devices * fetch_cap * tile_side, feat_width),
        (((0,), (0,)), ((), ())),
        preferred_element_type=jnp.float32,
    )
    grad_weight, grad_bias = all_sum(weight_term, bias_term)
    owned_sums = lax.psum_scatter(
        dense_rows, "row", scatter_dimension=0, tiled=True
    ).astype(jnp.float32)
    grad_proj = owned_sums.reshape(node_rows, feat_width).astype(jnp.bfloat16)
    grad_features = jnp.dot(grad_proj, weight.T, preferred_element_type=jnp.float32).astype(
        jnp.bfloat16
    )
    grad_scale = 1.0 / math.sqrt(node_rows * row_devices * col_devices)
    return (layer_out, grad_features, grad_weight * grad_scale, grad_bias * grad_scale)


def solution(mesh):
    return jax.shard_map(
        body,
        mesh=mesh,
        in_specs=(
            P(("row", "col"), None),
            P(),
            P(),
            P(("row", "col"), None, None),
            P(("row", "col")),
            P(("row", "col")),
            P(("row", "col")),
            P(("row", "col"), None),
            P(("row", "col"), None),
            P(("row", "col"), None),
        ),
        out_specs=(P(("row", "col"), None), P(("row", "col"), None), P(), P()),
        check_vma=False,
    )
```

```python
import functools
import math

import jax
import jax.numpy as jnp
from jax import lax
from jax.experimental import pallas as pl
from jax.experimental.pallas import tpu as pltpu
from jax.sharding import PartitionSpec as P


def silu_grad(values):
    logistic = jax.nn.sigmoid(values)
    return logistic * (1.0 + values * (1.0 - logistic))


def tile_kernel(take_ref, put_ref, count_ref, adj_ref, operand_ref, out_ref, acc_ref, *, transpose):
    acc_ref[...] = jnp.zeros_like(acc_ref)

    def step(k, carry):
        tile = adj_ref[k]
        picked = operand_ref[take_ref[k]]
        if transpose:
            product = lax.dot_general(
                tile, picked, (((0,), (0,)), ((), ())), preferred_element_type=jnp.float32
            )
        else:
            product = jnp.dot(tile, picked, preferred_element_type=jnp.float32)
        slot = put_ref[k]
        acc_ref[slot] = acc_ref[slot] + product
        return carry

    lax.fori_loop(0, count_ref[0], step, 0)
    out_ref[...] = acc_ref[...].astype(out_ref.dtype)


def tile_sums(adj_tiles, operand, take_slot, put_slot, live_count, slot_total, transpose):
    tile_side = adj_tiles.shape[1]
    width = operand.shape[-1]
    smem = pl.BlockSpec(memory_space=pltpu.SMEM)
    vmem = pl.BlockSpec(memory_space=pltpu.VMEM)
    flops = 2 * adj_tiles.shape[0] * tile_side * tile_side * width
    moved = (adj_tiles.size + operand.size + slot_total * tile_side * width) * 2
    return pl.pallas_call(
        functools.partial(tile_kernel, transpose=transpose),
        out_shape=jax.ShapeDtypeStruct((slot_total, tile_side, width), jnp.bfloat16),
        in_specs=[smem, smem, smem, vmem, vmem],
        out_specs=vmem,
        scratch_shapes=[pltpu.VMEM((slot_total, tile_side, width), jnp.float32)],
        compiler_params=pltpu.CompilerParams(vmem_limit_bytes=56 * 1024 * 1024),
        cost_estimate=pl.CostEstimate(flops=flops, bytes_accessed=moved, transcendentals=0),
    )(
        take_slot.astype(jnp.int32),
        put_slot.astype(jnp.int32),
        jnp.reshape(live_count, (1,)).astype(jnp.int32),
        adj_tiles,
        operand,
    )


def slot_add_kernel(put_ref, operand_ref, out_ref):
    out_ref[...] = jnp.zeros_like(out_ref)

    def step(s, carry):
        block = put_ref[s]
        out_ref[block] = out_ref[block] + operand_ref[s].astype(jnp.float32)
        return carry

    lax.fori_loop(0, operand_ref.shape[0], step, 0)


def slot_add(operand, put_block, block_total):
    tile_side, width = operand.shape[1:]
    smem = pl.BlockSpec(memory_space=pltpu.SMEM)
    vmem = pl.BlockSpec(memory_space=pltpu.VMEM)
    summed = pl.pallas_call(
        slot_add_kernel,
        out_shape=jax.ShapeDtypeStruct((block_total + 1, tile_side, width), jnp.float32),
        in_specs=[smem, vmem],
        out_specs=vmem,
        compiler_params=pltpu.CompilerParams(vmem_limit_bytes=32 * 1024 * 1024),
        cost_estimate=pl.CostEstimate(
            flops=operand.size,
            bytes_accessed=operand.size * 2 + (block_total + 1) * tile_side * width * 4,
            transcendentals=0,
        ),
    )(put_block.astype(jnp.int32), operand)
    return summed[:block_total]


def slot_take_kernel(take_ref, source_ref, out_ref):
    def step(s, carry):
        out_ref[s] = source_ref[take_ref[s]]
        return carry

    lax.fori_loop(0, out_ref.shape[0], step, 0)


def slot_take(source, take_block):
    slots = take_block.shape[0]
    smem = pl.BlockSpec(memory_space=pltpu.SMEM)
    vmem = pl.BlockSpec(memory_space=pltpu.VMEM)
    return pl.pallas_call(
        slot_take_kernel,
        out_shape=jax.ShapeDtypeStruct((slots,) + source.shape[1:], source.dtype),
        in_specs=[smem, vmem],
        out_specs=vmem,
        compiler_params=pltpu.CompilerParams(vmem_limit_bytes=32 * 1024 * 1024),
        cost_estimate=pl.CostEstimate(
            flops=0,
            bytes_accessed=(source.size + slots * source[0].size) * source.dtype.itemsize,
            transcendentals=0,
        ),
    )(take_block.astype(jnp.int32), source)


def all_sum(weight_term, bias_term):
    devices = lax.axis_size(("row", "col"))
    rows, width = weight_term.shape
    packed = jnp.concatenate([weight_term, bias_term[None, :]], axis=0)
    chunk = -(-(rows + 1) // devices)
    packed = jnp.pad(packed, ((0, chunk * devices - rows - 1), (0, 0)))
    parts = lax.all_to_all(
        packed.reshape(devices, chunk, width), ("row", "col"), 0, 0, tiled=True
    )
    owned = jnp.sum(parts, axis=0)
    spread = lax.all_to_all(
        jnp.broadcast_to(owned[None], (devices, chunk, width)), ("row", "col"), 0, 0, tiled=True
    ).reshape(devices * chunk, width)
    return spread[:rows], spread[rows]


def body(
    features,
    weight,
    layer_bias,
    adj_tiles,
    tile_source,
    tile_target,
    tile_count,
    fetch_list,
    deliver_list,
    cotangent,
):
    row_devices = lax.axis_size("row")
    col_devices = lax.axis_size("col")
    node_rows, feat_width = features.shape
    tile_side = adj_tiles.shape[1]
    own_blocks = node_rows // tile_side
    fetch_cap = fetch_list.shape[1]
    deliver_cap = deliver_list.shape[1]
    block_cells = tile_side * feat_width
    live_count = tile_count[0]
    column_features = lax.all_gather(features, "row", axis=0, tiled=True)
    column = jnp.dot(column_features, weight, preferred_element_type=jnp.float32).astype(
        jnp.bfloat16
    )
    source_operand = column.reshape(row_devices * own_blocks, tile_side, feat_width)
    global_ids = (
        jnp.arange(row_devices, dtype=jnp.int32)[:, None] * own_blocks + jnp.maximum(fetch_list, 0)
    ).reshape(-1)
    take_src = global_ids[tile_source]
    row_sums = tile_sums(
        adj_tiles,
        source_operand,
        take_src,
        tile_target,
        live_count,
        col_devices * deliver_cap,
        False,
    )
    outgoing_rows = row_sums.reshape(
        col_devices, deliver_cap, tile_side, feat_width
    )
    incoming = lax.all_to_all(outgoing_rows, "col", split_axis=0, concat_axis=0, tiled=True)
    deliver_flat = deliver_list.reshape(-1)
    aggregated = slot_add(
        incoming.reshape(col_devices * deliver_cap, tile_side, feat_width),
        jnp.where(deliver_flat >= 0, deliver_flat, own_blocks),
        own_blocks,
    )
    pre_act = aggregated.reshape(node_rows, feat_width) + layer_bias
    layer_out = jax.nn.silu(pre_act).astype(jnp.bfloat16)
    slopes = cotangent.astype(jnp.float32) * silu_grad(pre_act)
    bias_term = jnp.sum(slopes, axis=0)
    slope_blocks = slopes.astype(jnp.bfloat16).reshape(own_blocks, tile_side, feat_width)
    wanted_rows = slot_take(slope_blocks, jnp.maximum(deliver_flat, 0)).reshape(
        col_devices, deliver_cap, tile_side, feat_width
    )
    row_values = lax.all_to_all(
        wanted_rows, "col", split_axis=0, concat_axis=0, tiled=True
    ).reshape(col_devices * deliver_cap, tile_side, feat_width)
    src_sums = tile_sums(
        adj_tiles, row_values, tile_target, tile_source, live_count, row_devices * fetch_cap, True
    )
    rounded = src_sums.reshape(row_devices * fetch_cap, block_cells)
    valid_slots = fetch_list.reshape(-1) >= 0
    onehot = (
        (global_ids[None, :] == jnp.arange(row_devices * own_blocks, dtype=jnp.int32)[:, None])
        & valid_slots[None, :]
    ).astype(jnp.bfloat16)
    dense_rows = jnp.dot(onehot, rounded, preferred_element_type=jnp.float32).astype(jnp.bfloat16)
    slot_features = column_features.reshape(row_devices * own_blocks, tile_side, feat_width)[
        global_ids
    ]
    weight_term = lax.dot_general(
        slot_features.reshape(row_devices * fetch_cap * tile_side, feat_width),
        src_sums.reshape(row_devices * fetch_cap * tile_side, feat_width),
        (((0,), (0,)), ((), ())),
        preferred_element_type=jnp.float32,
    )
    grad_weight, grad_bias = all_sum(weight_term, bias_term)
    owned_sums = lax.psum_scatter(
        dense_rows, "row", scatter_dimension=0, tiled=True
    ).astype(jnp.float32)
    grad_proj = owned_sums.reshape(node_rows, feat_width).astype(jnp.bfloat16)
    grad_features = jnp.dot(grad_proj, weight.T, preferred_element_type=jnp.float32).astype(
        jnp.bfloat16
    )
    grad_scale = 1.0 / math.sqrt(node_rows * row_devices * col_devices)
    return (layer_out, grad_features, grad_weight * grad_scale, grad_bias * grad_scale)


def solution(mesh):
    return jax.shard_map(
        body,
        mesh=mesh,
        in_specs=(
            P(("row", "col"), None),
            P(),
            P(),
            P(("row", "col"), None, None),
            P(("row", "col")),
            P(("row", "col")),
            P(("row", "col")),
            P(("row", "col"), None),
            P(("row", "col"), None),
            P(("row", "col"), None),
        ),
        out_specs=(P(("row", "col"), None), P(("row", "col"), None), P(), P()),
        check_vma=False,
    )
```

```python
import functools
import math

import jax
import jax.numpy as jnp
from jax import lax
from jax.experimental import pallas as pl
from jax.experimental.pallas import tpu as pltpu
from jax.sharding import PartitionSpec as P


def silu_grad(values):
    logistic = jax.nn.sigmoid(values)
    return logistic * (1.0 + values * (1.0 - logistic))


def tile_kernel(order_ref, take_ref, put_ref, count_ref, adj_ref, operand_ref, out_ref, acc_ref, *, transpose):
    out_ref[...] = jnp.zeros_like(out_ref)
    count = count_ref[0]

    def step(i, carry):
        k = order_ref[i]
        tile = adj_ref[k]
        picked = operand_ref[take_ref[k]]
        if transpose:
            product = lax.dot_general(
                tile, picked, (((0,), (0,)), ((), ())), preferred_element_type=jnp.float32
            )
        else:
            product = jnp.dot(tile, picked, preferred_element_type=jnp.float32)
        slot = put_ref[k]
        previous = put_ref[order_ref[jnp.maximum(i - 1, 0)]]
        following = put_ref[order_ref[jnp.minimum(i + 1, count - 1)]]
        first = jnp.logical_or(i == 0, previous != slot)
        last = jnp.logical_or(i == count - 1, following != slot)

        @pl.when(first)
        def _():
            acc_ref[...] = product

        @pl.when(jnp.logical_not(first))
        def _():
            acc_ref[...] = acc_ref[...] + product

        @pl.when(last)
        def _():
            out_ref[slot] = acc_ref[...].astype(out_ref.dtype)

        return carry

    lax.fori_loop(0, count, step, 0)


def tile_sums(adj_tiles, operand, take_slot, put_slot, live_count, slot_total, transpose):
    tile_total, tile_side = adj_tiles.shape[:2]
    width = operand.shape[-1]
    put_slot = put_slot.astype(jnp.int32)
    live = jnp.arange(tile_total, dtype=jnp.int32) < live_count
    order = jnp.argsort(jnp.where(live, put_slot, slot_total), stable=True).astype(jnp.int32)
    smem = pl.BlockSpec(memory_space=pltpu.SMEM)
    vmem = pl.BlockSpec(memory_space=pltpu.VMEM)
    flops = 2 * tile_total * tile_side * tile_side * width
    moved = (adj_tiles.size + operand.size + slot_total * tile_side * width) * 2
    return pl.pallas_call(
        functools.partial(tile_kernel, transpose=transpose),
        out_shape=jax.ShapeDtypeStruct((slot_total, tile_side, width), jnp.bfloat16),
        in_specs=[smem, smem, smem, smem, vmem, vmem],
        out_specs=vmem,
        scratch_shapes=[pltpu.VMEM((tile_side, width), jnp.float32)],
        compiler_params=pltpu.CompilerParams(vmem_limit_bytes=56 * 1024 * 1024),
        cost_estimate=pl.CostEstimate(flops=flops, bytes_accessed=moved, transcendentals=0),
    )(
        order,
        take_slot.astype(jnp.int32),
        put_slot,
        jnp.reshape(live_count, (1,)).astype(jnp.int32),
        adj_tiles,
        operand,
    )


def slot_add_kernel(put_ref, operand_ref, out_ref):
    out_ref[...] = jnp.zeros_like(out_ref)

    def step(s, carry):
        block = put_ref[s]
        out_ref[block] = out_ref[block] + operand_ref[s].astype(jnp.float32)
        return carry

    lax.fori_loop(0, operand_ref.shape[0], step, 0)


def slot_add(operand, put_block, block_total):
    tile_side, width = operand.shape[1:]
    smem = pl.BlockSpec(memory_space=pltpu.SMEM)
    vmem = pl.BlockSpec(memory_space=pltpu.VMEM)
    summed = pl.pallas_call(
        slot_add_kernel,
        out_shape=jax.ShapeDtypeStruct((block_total + 1, tile_side, width), jnp.float32),
        in_specs=[smem, vmem],
        out_specs=vmem,
        compiler_params=pltpu.CompilerParams(vmem_limit_bytes=32 * 1024 * 1024),
        cost_estimate=pl.CostEstimate(
            flops=operand.size,
            bytes_accessed=operand.size * 2 + (block_total + 1) * tile_side * width * 4,
            transcendentals=0,
        ),
    )(put_block.astype(jnp.int32), operand)
    return summed[:block_total]


def slot_take_kernel(take_ref, source_ref, out_ref):
    def step(s, carry):
        out_ref[s] = source_ref[take_ref[s]]
        return carry

    lax.fori_loop(0, out_ref.shape[0], step, 0)


def slot_take(source, take_block):
    slots = take_block.shape[0]
    smem = pl.BlockSpec(memory_space=pltpu.SMEM)
    vmem = pl.BlockSpec(memory_space=pltpu.VMEM)
    return pl.pallas_call(
        slot_take_kernel,
        out_shape=jax.ShapeDtypeStruct((slots,) + source.shape[1:], source.dtype),
        in_specs=[smem, vmem],
        out_specs=vmem,
        compiler_params=pltpu.CompilerParams(vmem_limit_bytes=32 * 1024 * 1024),
        cost_estimate=pl.CostEstimate(
            flops=0,
            bytes_accessed=(source.size + slots * source[0].size) * source.dtype.itemsize,
            transcendentals=0,
        ),
    )(take_block.astype(jnp.int32), source)


def all_sum(weight_term, bias_term):
    devices = lax.axis_size(("row", "col"))
    rows, width = weight_term.shape
    packed = jnp.concatenate([weight_term, bias_term[None, :]], axis=0)
    chunk = -(-(rows + 1) // devices)
    packed = jnp.pad(packed, ((0, chunk * devices - rows - 1), (0, 0)))
    parts = lax.all_to_all(
        packed.reshape(devices, chunk, width), ("row", "col"), 0, 0, tiled=True
    )
    owned = jnp.sum(parts, axis=0)
    spread = lax.all_to_all(
        jnp.broadcast_to(owned[None], (devices, chunk, width)), ("row", "col"), 0, 0, tiled=True
    ).reshape(devices * chunk, width)
    return spread[:rows], spread[rows]


def body(
    features,
    weight,
    layer_bias,
    adj_tiles,
    tile_source,
    tile_target,
    tile_count,
    fetch_list,
    deliver_list,
    cotangent,
):
    row_devices = lax.axis_size("row")
    col_devices = lax.axis_size("col")
    node_rows, feat_width = features.shape
    tile_side = adj_tiles.shape[1]
    own_blocks = node_rows // tile_side
    fetch_cap = fetch_list.shape[1]
    deliver_cap = deliver_list.shape[1]
    block_cells = tile_side * feat_width
    live_count = tile_count[0]
    column_features = lax.all_gather(features, "row", axis=0, tiled=True)
    column = jnp.dot(column_features, weight, preferred_element_type=jnp.float32).astype(
        jnp.bfloat16
    )
    source_operand = column.reshape(row_devices * own_blocks, tile_side, feat_width)
    global_ids = (
        jnp.arange(row_devices, dtype=jnp.int32)[:, None] * own_blocks + jnp.maximum(fetch_list, 0)
    ).reshape(-1)
    take_src = global_ids[tile_source]
    row_sums = tile_sums(
        adj_tiles,
        source_operand,
        take_src,
        tile_target,
        live_count,
        col_devices * deliver_cap,
        False,
    )
    outgoing_rows = row_sums.reshape(
        col_devices, deliver_cap, tile_side, feat_width
    )
    incoming = lax.all_to_all(outgoing_rows, "col", split_axis=0, concat_axis=0, tiled=True)
    deliver_flat = deliver_list.reshape(-1)
    aggregated = slot_add(
        incoming.reshape(col_devices * deliver_cap, tile_side, feat_width),
        jnp.where(deliver_flat >= 0, deliver_flat, own_blocks),
        own_blocks,
    )
    pre_act = aggregated.reshape(node_rows, feat_width) + layer_bias
    layer_out = jax.nn.silu(pre_act).astype(jnp.bfloat16)
    slopes = cotangent.astype(jnp.float32) * silu_grad(pre_act)
    bias_term = jnp.sum(slopes, axis=0)
    slope_blocks = slopes.astype(jnp.bfloat16).reshape(own_blocks, tile_side, feat_width)
    wanted_rows = slot_take(slope_blocks, jnp.maximum(deliver_flat, 0)).reshape(
        col_devices, deliver_cap, tile_side, feat_width
    )
    row_values = lax.all_to_all(
        wanted_rows, "col", split_axis=0, concat_axis=0, tiled=True
    ).reshape(col_devices * deliver_cap, tile_side, feat_width)
    src_sums = tile_sums(
        adj_tiles, row_values, tile_target, tile_source, live_count, row_devices * fetch_cap, True
    )
    rounded = src_sums.reshape(row_devices * fetch_cap, block_cells)
    valid_slots = fetch_list.reshape(-1) >= 0
    onehot = (
        (global_ids[None, :] == jnp.arange(row_devices * own_blocks, dtype=jnp.int32)[:, None])
        & valid_slots[None, :]
    ).astype(jnp.bfloat16)
    dense_rows = jnp.dot(onehot, rounded, preferred_element_type=jnp.float32).astype(jnp.bfloat16)
    slot_features = column_features.reshape(row_devices * own_blocks, tile_side, feat_width)[
        global_ids
    ]
    weight_term = lax.dot_general(
        slot_features.reshape(row_devices * fetch_cap * tile_side, feat_width),
        src_sums.reshape(row_devices * fetch_cap * tile_side, feat_width),
        (((0,), (0,)), ((), ())),
        preferred_element_type=jnp.float32,
    )
    grad_weight, grad_bias = all_sum(weight_term, bias_term)
    owned_sums = lax.psum_scatter(
        dense_rows, "row", scatter_dimension=0, tiled=True
    ).astype(jnp.float32)
    grad_proj = owned_sums.reshape(node_rows, feat_width).astype(jnp.bfloat16)
    grad_features = jnp.dot(grad_proj, weight.T, preferred_element_type=jnp.float32).astype(
        jnp.bfloat16
    )
    grad_scale = 1.0 / math.sqrt(node_rows * row_devices * col_devices)
    return (layer_out, grad_features, grad_weight * grad_scale, grad_bias * grad_scale)


def solution(mesh):
    return jax.shard_map(
        body,
        mesh=mesh,
        in_specs=(
            P(("row", "col"), None),
            P(),
            P(),
            P(("row", "col"), None, None),
            P(("row", "col")),
            P(("row", "col")),
            P(("row", "col")),
            P(("row", "col"), None),
            P(("row", "col"), None),
            P(("row", "col"), None),
        ),
        out_specs=(P(("row", "col"), None), P(("row", "col"), None), P(), P()),
        check_vma=False,
    )
```
